256 devices in a mesh: dp: 4 (over y), expert: 64 (over x, z, core).
Axes of the slice: x: 4, y: 4, z: 8, core: 2. Of those that a mesh axis runs over, the one named last changes fastest.
Arguments:
- tokens: bfloat16 [2, 512, 7168], P(None, ('dp', 'expert')), parts along dimension 1, may hold values from -6 to 6
- expert_ids: int32 [2, 512, 8], P(None, ('dp', 'expert')), parts along dimension 1, may hold values from 0 to 15, all different within a row; in each aligned block of 2 rows (0 to 1, 2 to 3, ..., all dimensions but the last counted through in order) at most 2 rows name the same one
- gate_codes: int32 [2, 512, 8], P(None, ('dp', 'expert')), parts along dimension 1, may hold values from 1 to 1024
- w_gate: bfloat16 [256, 7168, 256], P(('dp', 'expert')), parts along dimension 0, may hold values from -0.0625 to 0.0625
- w_up: bfloat16 [256, 7168, 256], P(('dp', 'expert')), parts along dimension 0, may hold values from -0.0625 to 0.0625
- w_down: bfloat16 [256, 256, 7168], P(('dp', 'expert')), parts along dimension 0, may hold values from -0.1875 to 0.1875
Outputs:
- mixed: bfloat16 [2, 512, 7168], P(None, ('dp', 'expert')), parts along dimension 1
The draws below stay inside these ranges and needn't reach their ends.
There are 4 independent parts, one for each index of `dp`. The reference program is written for one: setup_inputs(seed, part) draws one part's arguments, and reference() takes and returns one part's arrays. A program takes and returns all parts, laid end to end along the dimension named above; each array names one. Nothing has to cross between parts.
Inputs may be any that keep to these rules, and one draw needn't show every extreme that they name: `expert_ids`: each row names 8 different experts. In each step, the 2 rows of one device name no expert more than 2 times, and in every draw some such block names some expert exactly 2 times.
All inputs are finite; a program needn't handle non-finite values.
Results may differ from the reference program's by a relative error of at most 0.0058.
Values may be sent and summed in bfloat16 or wider, within the bound.
No kernel may reach another device: no remote copies, remote signals or barrier semaphores. Data moves between devices by JAX's collectives and lax.ppermute only.
A program may use at most 64 MiB of HBM per device.

```python
import math
import jax
import jax.numpy as jnp
import numpy as np
from jax import lax

D = 7168
EH = 1024
HS = 256
ROWS_DEV = 2
STEPS = 2
SLICES = 64
GROUP = 4
EXPERTS = 16
TOP = 8
TOKENS = 128
CAP = 2
N_EXPERT = 64


def touch_ends(drawn, rng, least, top_value):
    spot = [jax.random.randint(jax.random.fold_in(rng, axis), (), 0, length) for axis, length in enumerate(drawn.shape)]
    widest = drawn.shape.index(max(drawn.shape))
    next_to = spot[:widest] + [(spot[widest] + 1) % drawn.shape[widest]] + spot[widest + 1:]
    return drawn.at[tuple(spot)].set(least).at[tuple(next_to)].set(top_value)


def block_levels(rng, dims, pieces, least, largest):
    loudness, own = 1.0, jax.random.fold_in(rng, 6)
    for position, shards_of in pieces:
        steps = jnp.exp(jax.random.uniform(jax.random.fold_in(own, position), (shards_of,), jnp.float32, least / len(pieces), largest / len(pieces)))
        loudness = loudness * jnp.repeat(steps, dims[position] // shards_of).reshape([-1 if axis == position else 1 for axis in range(len(dims))])
    return loudness


def shared_out(key, own, number, rows, count, top, reach, slope):
    ranking = jax.random.permutation(key, count)
    crowded, ordinary = shares(count, rows * top, reach, slope, True), shares(count, rows * top, reach, slope, False)
    places = jnp.arange(count)

    def named(tallies, offset_by):
        used = int((tallies > 0).sum())
        fixed = max(1, used // 4)
        passed = fixed + (places - fixed + offset_by * (used - fixed)) % max(1, count - fixed)
        return jnp.zeros((count,), jnp.int32).at[ranking[jnp.where(places < fixed, places, passed)]].set(jnp.asarray(tallies, jnp.int32))

    tallies = jnp.where(number % 4 == 0, named(crowded, number // 4), named(ordinary, number - number // 4 - 1))
    mixed = jax.random.permutation(jax.random.fold_in(own, 3), count)
    giver, sink = mixed[0:count // 2 * 2:2], mixed[1:count // 2 * 2:2]
    room = jnp.minimum(tallies[giver] - 1, reach - tallies[sink]) // 2
    room = jnp.where((giver == ranking[0]) | (sink == ranking[0]) | (tallies[sink] == 0), 0, jnp.maximum(room, 0))
    passed = jax.random.randint(jax.random.fold_in(own, 4), (count // 2,), 0, 1 << 20) % (room + 1)
    tallies = tallies.at[giver].add(-passed).at[sink].add(passed)
    members = jnp.searchsorted(jnp.cumsum(tallies), jnp.arange(rows * top), side="right").astype(jnp.int32)
    table = members.reshape(top, rows).T
    table = table[jax.random.permutation(jax.random.fold_in(own, 1), rows)]
    offset_by = jax.random.randint(jax.random.fold_in(own, 2), (rows, 1), 0, top)
    return jnp.take_along_axis(table, (jnp.arange(top)[None, :] + offset_by) % top, axis=1)


def shares(amount, total, reach, slope, full):
    portions = [(1 << 20) // math.isqrt(grade ** slope) + 1 for grade in range(1, amount + 1)]
    largest = reach if full else min(reach, max(-(-total // amount), total * portions[0] // sum(portions)))
    least = 1 if total - largest >= amount - 1 else 0
    counts, spare = [largest] + [least] * (amount - 1), total - largest - least * (amount - 1)
    while spare > 0:
        candidates = [i for i in range(1, amount) if counts[i] < largest] or [i for i in range(1, amount) if counts[i] < reach]
        pool, remaining = sum([portions[i] for i in candidates]), spare
        for i in candidates:
            more = min(reach - counts[i], max(1, remaining * portions[i] // pool), spare)
            counts[i] = counts[i] + more
            spare = spare - more
    return np.array(counts)


def normal_values(stream_key, shape, width, most, shards=(), kind=jnp.bfloat16):
    result = jax.random.normal(stream_key, shape, jnp.float32) * width
    if len(shards) > 0:
        result = block_levels(stream_key, shape, shards, -0.22, 0.18) * result
    return jnp.clip(result, min=-most, max=most).astype(kind)


def setup_inputs(seed: int = 0, part: int = 0) -> dict:
    key_list = jax.random.split(jax.random.key(seed), 7)
    own_keys = jax.random.split(jax.random.fold_in(key_list[6], part), 7)
    tokens = normal_values(own_keys[0], (STEPS, TOKENS, D), 1.0, 6.0, ((1, 64),))
    expert_ids_keys = jax.random.split(jax.random.fold_in(own_keys[1], 1), STEPS * TOKENS // ROWS_DEV)
    expert_ids_turns = jax.random.permutation(jax.random.fold_in(own_keys[1], 3), STEPS * TOKENS // ROWS_DEV)
    expert_ids = jax.vmap(lambda own, number: shared_out(jax.random.fold_in(own_keys[1], 2), own, number, ROWS_DEV, EXPERTS, TOP, CAP, 2))(expert_ids_keys, expert_ids_turns).reshape((STEPS, TOKENS, TOP))
    gate_codes = touch_ends(jax.random.randint(own_keys[2], (STEPS, TOKENS, TOP), 1, 1025), jax.random.fold_in(own_keys[2], 1), 1, 1024).astype(jnp.int32)
    w_gate = normal_values(own_keys[3], (SLICES, D, HS), D ** -0.5, 0.0625, ((0, 64),))
    w_up = normal_values(own_keys[4], (SLICES, D, HS), D ** -0.5, 0.0625, ((0, 64),))
    w_down = normal_values(own_keys[5], (SLICES, HS, D), EH ** -0.5, 0.1875, ((0, 64),))
    return {"tokens": tokens, "expert_ids": expert_ids, "gate_codes": gate_codes, "w_gate": w_gate, "w_up": w_up, "w_down": w_down}


def one_step(step_rows, step_ids, step_codes, w_gate, w_up, w_down):
    blocks = step_ids.reshape(N_EXPERT, ROWS_DEV * TOP)
    onehot = (blocks[:, :, None] == jnp.arange(EXPERTS, dtype=jnp.int32)[None, None, :]).astype(jnp.int32)
    slot_rank = jnp.sum(jnp.cumsum(onehot, 1) * onehot, -1) - 1
    block_index = jnp.broadcast_to(jnp.arange(N_EXPERT, dtype=jnp.int32)[:, None], blocks.shape)
    token_index = block_index * ROWS_DEV + (jnp.arange(ROWS_DEV * TOP, dtype=jnp.int32) // TOP)[None, :]
    slot_table = jnp.full((EXPERTS, N_EXPERT, CAP), TOKENS, jnp.int32)
    slot_table = slot_table.at[blocks, block_index, slot_rank].set(token_index)
    padded = jnp.concatenate([step_rows, jnp.zeros((1, D), jnp.bfloat16)], 0)

    def run_expert(expert):
        slot_rows = padded[slot_table[expert].reshape(-1)]
        total = jnp.zeros((slot_rows.shape[0], D), jnp.float32)
        for member in range(GROUP):
            block = expert * GROUP + member
            gate_act = jnp.dot(slot_rows, w_gate[block], preferred_element_type=jnp.float32)
            up_act = jnp.dot(slot_rows, w_up[block], preferred_element_type=jnp.float32)
            hidden = (jax.nn.silu(gate_act) * up_act).astype(jnp.bfloat16)
            partial_out = jnp.dot(hidden, w_down[block], preferred_element_type=jnp.float32).astype(jnp.bfloat16)
            total = total + partial_out.astype(jnp.float32)
        return total

    expert_out = lax.map(run_expert, jnp.arange(EXPERTS, dtype=jnp.int32))
    flat_slot = ((blocks * N_EXPERT + block_index) * CAP + slot_rank).reshape(TOKENS, TOP)
    picked = expert_out.reshape(-1, D)[flat_slot]
    codes = step_codes.astype(jnp.float32)
    gate_weight = codes / jnp.sum(codes, 1, keepdims=True)
    return jnp.sum(gate_weight[:, :, None] * picked, 1).astype(jnp.bfloat16)


def reference(tokens, expert_ids, gate_codes, w_gate, w_up, w_down):
    results = []
    for step in range(STEPS):
        results.append(one_step(tokens[step], expert_ids[step], gate_codes[step], w_gate, w_up, w_down))
    return jnp.stack(results, 0)
```

```python
import jax
import jax.numpy as jnp
import numpy as np
from jax import lax
from jax.sharding import Mesh
from jax.sharding import PartitionSpec as P

EH = 1024
HS = 256


def body(tokens, expert_ids, gate_codes, w_gate, w_up, w_down):
    step_count, row_count, width = tokens.shape
    group_size = EH // HS
    peer_count = lax.axis_size(("x", "z", "c"))
    experts_all = peer_count // group_size
    my_expert = lax.axis_index(("x", "z", "c")) // group_size

    codes = gate_codes.astype(jnp.float32)
    gate_weight = codes / jnp.sum(codes, -1, keepdims=True)
    onehot = expert_ids[..., None] == jnp.arange(experts_all, dtype=jnp.int32)
    table = jnp.sum(jnp.where(onehot, gate_weight[..., None], 0.0), -2)

    all_tokens = lax.all_gather(jnp.swapaxes(tokens, 0, 1), ("x", "z", "c"), axis=0, tiled=True)
    all_table = lax.all_gather(jnp.swapaxes(table, 0, 1), ("x", "z", "c"), axis=0, tiled=True)
    mine = jnp.arange(experts_all, dtype=jnp.int32) == my_expert
    scale = jnp.sum(jnp.where(mine, all_table, 0.0), -1)

    rows = all_tokens.reshape(-1, width)
    gate_act = jnp.dot(rows, w_gate[0], preferred_element_type=jnp.float32)
    up_act = jnp.dot(rows, w_up[0], preferred_element_type=jnp.float32)
    hidden = (jax.nn.silu(gate_act) * up_act).astype(jnp.bfloat16)
    partial_out = jnp.dot(hidden, w_down[0], preferred_element_type=jnp.float32).astype(
        jnp.bfloat16
    )
    contrib = partial_out.astype(jnp.float32) * scale.reshape(-1, 1)
    contrib = contrib.reshape(lax.axis_size(("x", "z")), lax.axis_size("c"), -1, width)
    contrib = jnp.swapaxes(contrib, 0, 1).reshape(-1, width)
    mixed = lax.psum_scatter(contrib, "c", scatter_dimension=0, tiled=True)
    mixed = lax.psum_scatter(mixed, ("x", "z"), scatter_dimension=0, tiled=True)
    mixed = lax.optimization_barrier(mixed)
    return jnp.swapaxes(mixed.reshape(-1, step_count, width), 0, 1).astype(jnp.bfloat16)


def solution(mesh):
    devices = np.asarray(mesh.devices)
    dp, expert = devices.shape
    chip_mesh = Mesh(devices.reshape(dp, 4, expert // 8, 2), ("dp", "x", "z", "c"))
    rows_spec = P(None, ("dp", "x", "z", "c"), None)
    blocks_spec = P(("dp", "x", "z", "c"), None, None)
    placed = (rows_spec, rows_spec, rows_spec, blocks_spec, blocks_spec, blocks_spec)
    return jax.shard_map(
        body, mesh=chip_mesh, in_specs=placed, out_specs=rows_spec, check_vma=False
    )
```

```python
import jax
import jax.numpy as jnp
from jax import lax
from jax.sharding import PartitionSpec as P

EH = 1024
HS = 256


def route_tables(step_ids, step_codes, experts_all, capacity):
    row_count, top_count = step_ids.shape
    flat_ids = step_ids.reshape(-1)
    onehot = (flat_ids[:, None] == jnp.arange(experts_all, dtype=jnp.int32)[None, :]).astype(
        jnp.int32
    )
    slot_rank = jnp.sum(jnp.cumsum(onehot, 0) * onehot, 1) - 1
    slot_index = flat_ids * capacity + slot_rank
    placement = slot_index[:, None] == jnp.arange(experts_all * capacity, dtype=jnp.int32)[None, :]
    codes = step_codes.astype(jnp.float32)
    gate_weight = codes / jnp.sum(codes, 1, keepdims=True)
    mix_table = jnp.sum(
        (placement.astype(jnp.float32) * gate_weight.reshape(-1)[:, None]).reshape(
            row_count, top_count, -1
        ),
        1,
    )
    return (placement, mix_table)


def body(tokens, expert_ids, gate_codes, w_gate, w_up, w_down):
    step_count, row_count, width = tokens.shape
    top_count = expert_ids.shape[2]
    peer_count = lax.axis_size("expert")
    group_size = EH // HS
    experts_all = peer_count // group_size
    capacity = min(row_count, max(2, 2 * row_count * top_count // experts_all))
    send_rows = []
    mix_tables = []
    for step in range(step_count):
        placement, mix_table = route_tables(
            expert_ids[step], gate_codes[step], experts_all, capacity
        )
        repeated = jnp.repeat(tokens[step], top_count, 0)
        slots = jnp.einsum(
            "as,ad->sd",
            placement.astype(jnp.bfloat16),
            repeated,
            preferred_element_type=jnp.float32,
        ).astype(jnp.bfloat16)
        send_rows.append(slots.reshape(experts_all, 1, capacity, width))
        mix_tables.append(mix_table)
    slots = jnp.repeat(jnp.concatenate(send_rows, 1), group_size, 0)
    received = lax.all_to_all(slots, "expert", split_axis=0, concat_axis=0, tiled=True)
    gate_act = jnp.einsum(
        "...cd,dh->...ch", received, w_gate[0], preferred_element_type=jnp.float32
    )
    up_act = jnp.einsum("...cd,dh->...ch", received, w_up[0], preferred_element_type=jnp.float32)
    hidden = (jax.nn.silu(gate_act) * up_act).astype(jnp.bfloat16)
    outputs_sent = jnp.einsum(
        "...ch,hd->...cd", hidden, w_down[0], preferred_element_type=jnp.float32
    ).astype(jnp.bfloat16)
    returned = lax.all_to_all(outputs_sent, "expert", split_axis=0, concat_axis=0, tiled=True)
    grouped = returned.reshape(experts_all, group_size, step_count, capacity, width).astype(
        jnp.float32
    )
    expert_out = jnp.sum(grouped, 1)
    results = []
    for step in range(step_count):
        combined = jnp.dot(
            mix_tables[step],
            expert_out[:, step].reshape(-1, width),
            precision=lax.Precision.HIGHEST,
            preferred_element_type=jnp.float32,
        )
        results.append(combined.astype(jnp.bfloat16))
    return jnp.stack(results, 0)


def solution(mesh):
    placed = (
        P(None, ("dp", "expert"), None),
        P(None, ("dp", "expert"), None),
        P(None, ("dp", "expert"), None),
        P(("dp", "expert"), None, None),
        P(("dp", "expert"), None, None),
        P(("dp", "expert"), None, None),
    )
    return jax.shard_map(
        body, mesh=mesh, in_specs=placed, out_specs=P(None, ("dp", "expert"), None), check_vma=False
    )
```

```python
import jax
import jax.numpy as jnp
import numpy as np
from jax import lax
from jax.sharding import Mesh
from jax.sharding import PartitionSpec as P

EH = 1024
HS = 256
CROSS = ("x", "zh")


def route_tables(step_ids, step_codes, experts_all, capacity):
    row_count, top_count = step_ids.shape
    flat_ids = step_ids.reshape(-1)
    onehot = (flat_ids[:, None] == jnp.arange(experts_all, dtype=jnp.int32)[None, :]).astype(
        jnp.int32
    )
    slot_rank = jnp.sum(jnp.cumsum(onehot, 0) * onehot, 1) - 1
    slot_index = flat_ids * capacity + slot_rank
    placement = slot_index[:, None] == jnp.arange(experts_all * capacity, dtype=jnp.int32)[None, :]
    codes = step_codes.astype(jnp.float32)
    gate_weight = codes / jnp.sum(codes, 1, keepdims=True)
    mix_table = jnp.sum(
        (placement.astype(jnp.float32) * gate_weight.reshape(-1)[:, None]).reshape(
            row_count, top_count, -1
        ),
        1,
    )
    return (placement, mix_table)


def swap(value, axis):
    return lax.ppermute(value, axis, [(0, 1), (1, 0)])


def body(tokens, expert_ids, gate_codes, w_gate, w_up, w_down):
    step_count, row_count, width = tokens.shape
    top_count = expert_ids.shape[2]
    experts_all = lax.axis_size(CROSS)
    capacity = min(row_count, max(2, 2 * row_count * top_count // experts_all))
    send_rows = []
    mix_tables = []
    for step in range(step_count):
        placement, mix_table = route_tables(
            expert_ids[step], gate_codes[step], experts_all, capacity
        )
        repeated = jnp.repeat(tokens[step], top_count, 0)
        slots = jnp.einsum(
            "as,ad->sd",
            placement.astype(jnp.bfloat16),
            repeated,
            preferred_element_type=jnp.float32,
        ).astype(jnp.bfloat16)
        send_rows.append(slots.reshape(experts_all, 1, capacity, width))
        mix_tables.append(mix_table)
    slots = jnp.concatenate(send_rows, 1)
    received = lax.all_to_all(slots, CROSS, split_axis=0, concat_axis=0, tiled=True)
    received = jnp.stack([received, swap(received, "zl")], 0)
    received = jnp.stack([received, swap(received, "c")], 0)
    gate_act = jnp.einsum(
        "...cd,dh->...ch", received, w_gate[0], preferred_element_type=jnp.float32
    )
    up_act = jnp.einsum("...cd,dh->...ch", received, w_up[0], preferred_element_type=jnp.float32)
    hidden = (jax.nn.silu(gate_act) * up_act).astype(jnp.bfloat16)
    partial_out = jnp.einsum(
        "...ch,hd->...cd", hidden, w_down[0], preferred_element_type=jnp.float32
    ).astype(jnp.bfloat16)
    chip_sum = partial_out[0].astype(jnp.float32) + swap(partial_out[1], "c").astype(jnp.float32)
    chip_sum = chip_sum.astype(jnp.bfloat16)
    expert_out = chip_sum[0].astype(jnp.float32) + swap(chip_sum[1], "zl").astype(jnp.float32)
    returned = lax.all_to_all(
        expert_out.astype(jnp.bfloat16), CROSS, split_axis=0, concat_axis=0, tiled=True
    ).astype(jnp.float32)
    results = []
    for step in range(step_count):
        combined = jnp.dot(
            mix_tables[step],
            returned[:, step].reshape(-1, width),
            precision=lax.Precision.HIGHEST,
            preferred_element_type=jnp.float32,
        )
        results.append(combined.astype(jnp.bfloat16))
    return jnp.stack(results, 0)


def solution(mesh):
    devices = np.asarray(mesh.devices)
    dp, expert = devices.shape
    chip_mesh = Mesh(
        devices.reshape(dp, 4, expert // 16, 2, 2), ("dp", "x", "zh", "zl", "c")
    )
    rows_spec = P(None, ("dp", "x", "zh", "zl", "c"), None)
    blocks_spec = P(("dp", "x", "zh", "zl", "c"), None, None)
    placed = (rows_spec, rows_spec, rows_spec, blocks_spec, blocks_spec, blocks_spec)
    return jax.shard_map(
        body, mesh=chip_mesh, in_specs=placed, out_specs=rows_spec, check_vma=False
    )
```

```python
import jax
import jax.numpy as jnp
import numpy as np
from jax import lax
from jax.sharding import Mesh
from jax.sharding import PartitionSpec as P

EH = 1024
HS = 256
CROSS = ("x", "zh")
SPREAD = ("x", "zh", "zl")


def swap(value, axis):
    return lax.ppermute(value, axis, [(0, 1), (1, 0)])


def body(tokens, expert_ids, gate_codes, w_gate, w_up, w_down):
    step_count, row_count, width = tokens.shape
    experts_all = lax.axis_size(CROSS)
    codes = gate_codes.astype(jnp.float32)
    gate_weight = codes / jnp.sum(codes, -1, keepdims=True)
    chosen = expert_ids[..., None] == jnp.arange(experts_all, dtype=jnp.int32)
    table = jnp.sum(jnp.where(chosen, gate_weight[..., None], 0.0), -2)

    gathered = lax.all_gather(tokens, SPREAD, axis=0, tiled=False)
    rows = jnp.stack([gathered, swap(gathered, "c")], 0)
    gate_act = jnp.einsum("...d,dh->...h", rows, w_gate[0], preferred_element_type=jnp.float32)
    up_act = jnp.einsum("...d,dh->...h", rows, w_up[0], preferred_element_type=jnp.float32)
    hidden = (jax.nn.silu(gate_act) * up_act).astype(jnp.bfloat16)
    partial_out = jnp.einsum(
        "...h,hd->...d", hidden, w_down[0], preferred_element_type=jnp.float32
    ).astype(jnp.bfloat16)
    chip_sum = partial_out[0].astype(jnp.float32) + swap(partial_out[1], "c").astype(jnp.float32)
    chip_sum = chip_sum.astype(jnp.bfloat16).reshape(experts_all, 2, step_count, row_count, width)
    my_zl = lax.axis_index("zl")
    own = lax.dynamic_index_in_dim(chip_sum, my_zl, 1, keepdims=False)
    other = lax.dynamic_index_in_dim(chip_sum, 1 - my_zl, 1, keepdims=False)
    expert_out = own.astype(jnp.float32) + swap(other, "zl").astype(jnp.float32)
    returned = lax.all_to_all(
        expert_out.astype(jnp.bfloat16), CROSS, split_axis=0, concat_axis=0, tiled=True
    ).astype(jnp.float32)
    weights = jnp.moveaxis(table, -1, 0)[..., None]
    mixed = jnp.sum(weights * returned, 0)
    return mixed.astype(jnp.bfloat16)


def solution(mesh):
    devices = np.asarray(mesh.devices)
    dp, expert = devices.shape
    chip_mesh = Mesh(
        devices.reshape(dp, 4, expert // 16, 2, 2), ("dp", "x", "zh", "zl", "c")
    )
    rows_spec = P(None, ("dp", "x", "zh", "zl", "c"), None)
    blocks_spec = P(("dp", "x", "zh", "zl", "c"), None, None)
    placed = (rows_spec, rows_spec, rows_spec, blocks_spec, blocks_spec, blocks_spec)
    return jax.shard_map(
        body, mesh=chip_mesh, in_specs=placed, out_specs=rows_spec, check_vma=False
    )
```

```python
import jax
import jax.numpy as jnp
import numpy as np
from jax import lax
from jax.sharding import Mesh
from jax.sharding import PartitionSpec as P

EH = 1024
HS = 256
CROSS = ("x", "zh")


def route_tables(step_ids, step_codes, experts_all, capacity):
    row_count, top_count = step_ids.shape
    flat_ids = step_ids.reshape(-1)
    onehot = (flat_ids[:, None] == jnp.arange(experts_all, dtype=jnp.int32)[None, :]).astype(
        jnp.int32
    )
    slot_rank = jnp.sum(jnp.cumsum(onehot, 0) * onehot, 1) - 1
    slot_index = flat_ids * capacity + slot_rank
    placement = slot_index[:, None] == jnp.arange(experts_all * capacity, dtype=jnp.int32)[None, :]
    codes = step_codes.astype(jnp.float32)
    gate_weight = codes / jnp.sum(codes, 1, keepdims=True)
    mix_table = jnp.sum(
        (placement.astype(jnp.float32) * gate_weight.reshape(-1)[:, None]).reshape(
            row_count, top_count, -1
        ),
        1,
    )
    return (placement, mix_table)


def swap(value, axis):
    return lax.ppermute(value, axis, [(0, 1), (1, 0)])


def shifted(index, offset, sizes, sign):
    coords = []
    for size in reversed(sizes):
        coords.append(index % size)
        index = index // size
    deltas = []
    for size in reversed(sizes):
        deltas.append(offset % size)
        offset = offset // size
    out = 0
    for size, coord, delta in zip(sizes, reversed(coords), reversed(deltas)):
        out = out * size + (coord + sign * delta) % size
    return out


def exchange(chunks, sizes, sign):
    count = int(np.prod(sizes))
    out = [chunks[0]]
    for offset in range(1, count):
        pairs = [(i, shifted(i, offset, sizes, sign)) for i in range(count)]
        out.append(lax.ppermute(chunks[offset], CROSS, pairs))
    return jnp.stack(out, 0)


def body(tokens, expert_ids, gate_codes, w_gate, w_up, w_down):
    step_count, row_count, width = tokens.shape
    top_count = expert_ids.shape[2]
    sizes = [lax.axis_size(name) for name in CROSS]
    experts_all = int(np.prod(sizes))
    capacity = min(row_count, max(2, 2 * row_count * top_count // experts_all))
    me = lax.axis_index(CROSS)
    targets = jnp.stack([shifted(me, o, sizes, 1) for o in range(experts_all)])
    send_rows = []
    mix_tables = []
    for step in range(step_count):
        placement, mix_table = route_tables(
            expert_ids[step], gate_codes[step], experts_all, capacity
        )
        repeated = jnp.repeat(tokens[step], top_count, 0)
        slots = jnp.einsum(
            "as,ad->sd",
            placement.astype(jnp.bfloat16),
            repeated,
            preferred_element_type=jnp.float32,
        ).astype(jnp.bfloat16)
        send_rows.append(slots.reshape(experts_all, 1, capacity, width))
        mix_tables.append(
            jnp.take(mix_table.reshape(row_count, experts_all, capacity), targets, axis=1)
        )
    slots = jnp.take(jnp.concatenate(send_rows, 1), targets, axis=0)
    received = exchange([slots[o] for o in range(experts_all)], sizes, 1)
    received = jnp.stack([received, swap(received, "zl")], 0)
    received = jnp.stack([received, swap(received, "c")], 0)
    gate_act = jnp.einsum(
        "...cd,dh->...ch", received, w_gate[0], preferred_element_type=jnp.float32
    )
    up_act = jnp.einsum("...cd,dh->...ch", received, w_up[0], preferred_element_type=jnp.float32)
    hidden = (jax.nn.silu(gate_act) * up_act).astype(jnp.bfloat16)
    partial_out = jnp.einsum(
        "...ch,hd->...cd", hidden, w_down[0], preferred_element_type=jnp.float32
    ).astype(jnp.bfloat16)
    chip_sum = partial_out[0].astype(jnp.float32) + swap(partial_out[1], "c").astype(jnp.float32)
    chip_sum = chip_sum.astype(jnp.bfloat16)
    expert_out = chip_sum[0].astype(jnp.float32) + swap(chip_sum[1], "zl").astype(jnp.float32)
    expert_out = expert_out.astype(jnp.bfloat16)
    returned = exchange([expert_out[o] for o in range(experts_all)], sizes, -1).astype(
        jnp.float32
    )
    results = []
    for step in range(step_count):
        combined = jnp.dot(
            mix_tables[step].reshape(row_count, -1),
            returned[:, step].reshape(-1, width),
            precision=lax.Precision.HIGHEST,
            preferred_element_type=jnp.float32,
        )
        results.append(combined.astype(jnp.bfloat16))
    return jnp.stack(results, 0)


def solution(mesh):
    devices = np.asarray(mesh.devices)
    dp, expert = devices.shape
    chip_mesh = Mesh(
        devices.reshape(dp, 4, expert // 16, 2, 2), ("dp", "x", "zh", "zl", "c")
    )
    rows_spec = P(None, ("dp", "x", "zh", "zl", "c"), None)
    blocks_spec = P(("dp", "x", "zh", "zl", "c"), None, None)
    placed = (rows_spec, rows_spec, rows_spec, blocks_spec, blocks_spec, blocks_spec)
    return jax.shard_map(
        body, mesh=chip_mesh, in_specs=placed, out_specs=rows_spec, check_vma=False
    )
```

```python
import jax
import jax.numpy as jnp
import numpy as np
from jax import lax
from jax.sharding import Mesh
from jax.sharding import PartitionSpec as P

EH = 1024
HS = 256
CROSS = ("x", "zh")
PAIRS = ("x", "zh", "zl")


def route_tables(step_ids, step_codes, experts_all, capacity):
    row_count, top_count = step_ids.shape
    flat_ids = step_ids.reshape(-1)
    onehot = (flat_ids[:, None] == jnp.arange(experts_all, dtype=jnp.int32)[None, :]).astype(
        jnp.int32
    )
    slot_rank = jnp.sum(jnp.cumsum(onehot, 0) * onehot, 1) - 1
    slot_index = flat_ids * capacity + slot_rank
    placement = slot_index[:, None] == jnp.arange(experts_all * capacity, dtype=jnp.int32)[None, :]
    codes = step_codes.astype(jnp.float32)
    gate_weight = codes / jnp.sum(codes, 1, keepdims=True)
    mix_table = jnp.sum(
        (placement.astype(jnp.float32) * gate_weight.reshape(-1)[:, None]).reshape(
            row_count, top_count, -1
        ),
        1,
    )
    return (placement, mix_table)


def swap(value, axis):
    return lax.ppermute(value, axis, [(0, 1), (1, 0)])


def body(tokens, expert_ids, gate_codes, w_gate, w_up, w_down):
    step_count, row_count, width = tokens.shape
    top_count = expert_ids.shape[2]
    experts_all = lax.axis_size(CROSS)
    capacity = min(row_count, max(2, 2 * row_count * top_count // experts_all))
    send_rows = []
    mix_tables = []
    for step in range(step_count):
        placement, mix_table = route_tables(
            expert_ids[step], gate_codes[step], experts_all, capacity
        )
        repeated = jnp.repeat(tokens[step], top_count, 0)
        slots = jnp.einsum(
            "as,ad->sd",
            placement.astype(jnp.bfloat16),
            repeated,
            preferred_element_type=jnp.float32,
        ).astype(jnp.bfloat16)
        send_rows.append(slots.reshape(experts_all, 1, capacity, width))
        mix_tables.append(mix_table)
    slots = jnp.repeat(jnp.concatenate(send_rows, 1), lax.axis_size("zl"), 0)
    received = lax.all_to_all(slots, PAIRS, split_axis=0, concat_axis=0, tiled=True)
    received = jnp.stack([received, swap(received, "c")], 0)
    gate_act = jnp.einsum(
        "...cd,dh->...ch", received, w_gate[0], preferred_element_type=jnp.float32
    )
    up_act = jnp.einsum("...cd,dh->...ch", received, w_up[0], preferred_element_type=jnp.float32)
    hidden = (jax.nn.silu(gate_act) * up_act).astype(jnp.bfloat16)
    partial_out = jnp.einsum(
        "...ch,hd->...cd", hidden, w_down[0], preferred_element_type=jnp.float32
    ).astype(jnp.bfloat16)
    chip_sum = partial_out[0].astype(jnp.float32) + swap(partial_out[1], "c").astype(jnp.float32)
    returned = lax.all_to_all(
        chip_sum.astype(jnp.bfloat16), PAIRS, split_axis=0, concat_axis=0, tiled=True
    ).astype(jnp.float32)
    returned = jnp.sum(returned.reshape(experts_all, -1, *returned.shape[1:]), 1)
    results = []
    for step in range(step_count):
        combined = jnp.dot(
            mix_tables[step],
            returned[:, step].reshape(-1, width),
            precision=lax.Precision.HIGHEST,
            preferred_element_type=jnp.float32,
        )
        results.append(combined.astype(jnp.bfloat16))
    return jnp.stack(results, 0)


def solution(mesh):
    devices = np.asarray(mesh.devices)
    dp, expert = devices.shape
    chip_mesh = Mesh(
        devices.reshape(dp, 4, expert // 16, 2, 2), ("dp", "x", "zh", "zl", "c")
    )
    rows_spec = P(None, ("dp", "x", "zh", "zl", "c"), None)
    blocks_spec = P(("dp", "x", "zh", "zl", "c"), None, None)
    placed = (rows_spec, rows_spec, rows_spec, blocks_spec, blocks_spec, blocks_spec)
    return jax.shard_map(
        body, mesh=chip_mesh, in_specs=placed, out_specs=rows_spec, check_vma=False
    )
```

```python
import jax
import jax.numpy as jnp
import numpy as np
from jax import lax
from jax.sharding import Mesh
from jax.sharding import PartitionSpec as P

EH = 1024
HS = 256
CROSS = ("x", "zh")
PAIRS = ("x", "zh", "zl")


def route_tables(step_ids, step_codes, experts_all, capacity):
    row_count, top_count = step_ids.shape
    flat_ids = step_ids.reshape(-1)
    onehot = (flat_ids[:, None] == jnp.arange(experts_all, dtype=jnp.int32)[None, :]).astype(
        jnp.int32
    )
    slot_rank = jnp.sum(jnp.cumsum(onehot, 0) * onehot, 1) - 1
    slot_index = flat_ids * capacity + slot_rank
    placement = slot_index[:, None] == jnp.arange(experts_all * capacity, dtype=jnp.int32)[None, :]
    codes = step_codes.astype(jnp.float32)
    gate_weight = codes / jnp.sum(codes, 1, keepdims=True)
    mix_table = jnp.sum(
        (placement.astype(jnp.float32) * gate_weight.reshape(-1)[:, None]).reshape(
            row_count, top_count, -1
        ),
        1,
    )
    return (placement, mix_table)


def swap(value, axis):
    return lax.ppermute(value, axis, [(0, 1), (1, 0)])


def body(tokens, expert_ids, gate_codes, w_gate, w_up, w_down):
    step_count, row_count, width = tokens.shape
    top_count = expert_ids.shape[2]
    experts_all = lax.axis_size(CROSS)
    capacity = min(row_count, max(2, 2 * row_count * top_count // experts_all))
    send_rows = []
    mix_tables = []
    for step in range(step_count):
        placement, mix_table = route_tables(
            expert_ids[step], gate_codes[step], experts_all, capacity
        )
        repeated = jnp.repeat(tokens[step], top_count, 0)
        chips = lax.axis_size("zl")
        placement = jnp.repeat(placement.reshape(-1, experts_all, 1, capacity), chips, 2)
        slots = jnp.einsum(
            "as,ad->sd",
            placement.reshape(placement.shape[0], -1).astype(jnp.bfloat16),
            repeated,
            preferred_element_type=jnp.float32,
        ).astype(jnp.bfloat16)
        send_rows.append(slots.reshape(experts_all * chips, 1, capacity, width))
        mix_table = jnp.repeat(mix_table.reshape(row_count, experts_all, 1, capacity), chips, 2)
        mix_tables.append(mix_table.reshape(row_count, -1))
    slots = jnp.concatenate(send_rows, 1)
    received = lax.all_to_all(slots, PAIRS, split_axis=0, concat_axis=0, tiled=True)
    received = jnp.stack([received, swap(received, "c")], 0)
    gate_act = jnp.einsum(
        "...cd,dh->...ch", received, w_gate[0], preferred_element_type=jnp.float32
    )
    up_act = jnp.einsum("...cd,dh->...ch", received, w_up[0], preferred_element_type=jnp.float32)
    hidden = (jax.nn.silu(gate_act) * up_act).astype(jnp.bfloat16)
    partial_out = jnp.einsum(
        "...ch,hd->...cd", hidden, w_down[0], preferred_element_type=jnp.float32
    ).astype(jnp.bfloat16)
    chip_sum = partial_out[0].astype(jnp.float32) + swap(partial_out[1], "c").astype(jnp.float32)
    returned = lax.all_to_all(
        chip_sum.astype(jnp.bfloat16), PAIRS, split_axis=0, concat_axis=0, tiled=True
    ).astype(jnp.float32)
    results = []
    for step in range(step_count):
        combined = jnp.dot(
            mix_tables[step],
            returned[:, step].reshape(-1, width),
            precision=lax.Precision.HIGHEST,
            preferred_element_type=jnp.float32,
        )
        results.append(combined.astype(jnp.bfloat16))
    return jnp.stack(results, 0)


def solution(mesh):
    devices = np.asarray(mesh.devices)
    dp, expert = devices.shape
    chip_mesh = Mesh(
        devices.reshape(dp, 4, expert // 16, 2, 2), ("dp", "x", "zh", "zl", "c")
    )
    rows_spec = P(None, ("dp", "x", "zh", "zl", "c"), None)
    blocks_spec = P(("dp", "x", "zh", "zl", "c"), None, None)
    placed = (rows_spec, rows_spec, rows_spec, blocks_spec, blocks_spec, blocks_spec)
    return jax.shard_map(
        body, mesh=chip_mesh, in_specs=placed, out_specs=rows_spec, check_vma=False
    )
```

```python
import jax
import jax.numpy as jnp
import numpy as np
from jax import lax
from jax.sharding import Mesh
from jax.sharding import PartitionSpec as P

EH = 1024
HS = 256
CROSS = ("x", "zh")


def route_tables(step_ids, step_codes, experts_all, capacity):
    row_count, top_count = step_ids.shape
    flat_ids = step_ids.reshape(-1)
    onehot = (flat_ids[:, None] == jnp.arange(experts_all, dtype=jnp.int32)[None, :]).astype(
        jnp.int32
    )
    slot_rank = jnp.sum(jnp.cumsum(onehot, 0) * onehot, 1) - 1
    slot_index = flat_ids * capacity + slot_rank
    placement = slot_index[:, None] == jnp.arange(experts_all * capacity, dtype=jnp.int32)[None, :]
    codes = step_codes.astype(jnp.float32)
    gate_weight = codes / jnp.sum(codes, 1, keepdims=True)
    mix_table = jnp.sum(
        (placement.astype(jnp.float32) * gate_weight.reshape(-1)[:, None]).reshape(
            row_count, top_count, -1
        ),
        1,
    )
    return (placement, mix_table)


def swap(value, axis):
    return lax.ppermute(value, axis, [(0, 1), (1, 0)])


def body(tokens, expert_ids, gate_codes, w_gate, w_up, w_down):
    step_count, row_count, width = tokens.shape
    top_count = expert_ids.shape[2]
    experts_all = lax.axis_size(CROSS)
    capacity = min(row_count, max(2, 2 * row_count * top_count // experts_all))
    send_rows = []
    mix_tables = []
    for step in range(step_count):
        placement, mix_table = route_tables(
            expert_ids[step], gate_codes[step], experts_all, capacity
        )
        repeated = jnp.repeat(tokens[step], top_count, 0)
        slots = jnp.einsum(
            "as,ad->sd",
            placement.astype(jnp.bfloat16),
            repeated,
            preferred_element_type=jnp.float32,
        ).astype(jnp.bfloat16)
        send_rows.append(slots.reshape(experts_all, 1, capacity, width))
        mix_tables.append(mix_table)
    slots = jnp.concatenate(send_rows, 1)
    received = lax.all_to_all(slots, CROSS, split_axis=0, concat_axis=0, tiled=True)
    received = jnp.stack([received, swap(received, "zl")], 0)
    received = jnp.stack([received, swap(received, "c")], 0)
    gate_act = jnp.einsum(
        "...cd,dh->...ch", received, w_gate[0], preferred_element_type=jnp.float32
    )
    up_act = jnp.einsum("...cd,dh->...ch", received, w_up[0], preferred_element_type=jnp.float32)
    hidden = (jax.nn.silu(gate_act) * up_act).astype(jnp.bfloat16)
    partial_out = jnp.einsum(
        "...ch,hd->...cd", hidden, w_down[0], preferred_element_type=jnp.float32
    ).astype(jnp.bfloat16)
    chip_sum = partial_out[0].astype(jnp.float32) + swap(partial_out[1], "c").astype(jnp.float32)
    expert_out = chip_sum[0] + swap(chip_sum[1].astype(jnp.bfloat16), "zl").astype(jnp.float32)
    returned = lax.all_to_all(
        expert_out.astype(jnp.bfloat16), CROSS, split_axis=0, concat_axis=0, tiled=True
    ).astype(jnp.float32)
    results = []
    for step in range(step_count):
        combined = jnp.dot(
            mix_tables[step],
            returned[:, step].reshape(-1, width),
            precision=lax.Precision.HIGHEST,
            preferred_element_type=jnp.float32,
        )
        results.append(combined.astype(jnp.bfloat16))
    return jnp.stack(results, 0)


def solution(mesh):
    devices = np.asarray(mesh.devices)
    dp, expert = devices.shape
    chip_mesh = Mesh(
        devices.reshape(dp, 4, expert // 16, 2, 2), ("dp", "x", "zh", "zl", "c")
    )
    rows_spec = P(None, ("dp", "x", "zh", "zl", "c"), None)
    blocks_spec = P(("dp", "x", "zh", "zl", "c"), None, None)
    placed = (rows_spec, rows_spec, rows_spec, blocks_spec, blocks_spec, blocks_spec)
    return jax.shard_map(
        body, mesh=chip_mesh, in_specs=placed, out_specs=rows_spec, check_vma=False
    )
```

```python
import jax
import jax.numpy as jnp
import numpy as np
from jax import lax
from jax.sharding import Mesh
from jax.sharding import PartitionSpec as P

EH = 1024
HS = 256
CROSS = ("x", "zh")


def route_tables(expert_ids, gate_codes, experts_all, capacity):
    step_count, row_count, top_count = expert_ids.shape
    flat = expert_ids.reshape(step_count, -1)
    order = jnp.arange(row_count * top_count, dtype=jnp.int32)
    earlier = order[None, :] < order[:, None]
    same = flat[:, :, None] == flat[:, None, :]
    slot_rank = jnp.sum(same & earlier, -1).reshape(expert_ids.shape)
    hit = (expert_ids[..., None, None] == jnp.arange(experts_all, dtype=jnp.int32)[:, None]) & (
        slot_rank[..., None, None] == jnp.arange(capacity, dtype=jnp.int32)
    )
    codes = gate_codes.astype(jnp.float32)
    gate_weight = codes / jnp.sum(codes, -1, keepdims=True)
    placement = jnp.sum(hit.astype(jnp.int32), 2)
    mix_table = jnp.sum(jnp.where(hit, gate_weight[..., None, None], 0.0), 2)
    return (placement, mix_table)


def swap(value, axis):
    return lax.ppermute(value, axis, [(0, 1), (1, 0)])


def body(tokens, expert_ids, gate_codes, w_gate, w_up, w_down):
    step_count, row_count, width = tokens.shape
    top_count = expert_ids.shape[2]
    experts_all = lax.axis_size(CROSS)
    capacity = min(row_count, max(2, 2 * row_count * top_count // experts_all))
    placement, mix_table = route_tables(expert_ids, gate_codes, experts_all, capacity)
    slots = jnp.einsum(
        "srec,srd->escd",
        placement.astype(jnp.bfloat16),
        tokens,
        preferred_element_type=jnp.float32,
    ).astype(jnp.bfloat16)
    received = lax.all_to_all(slots, CROSS, split_axis=0, concat_axis=0, tiled=True)
    received = jnp.stack([received, swap(received, "zl")], 0)
    received = jnp.stack([received, swap(received, "c")], 0)
    gate_act = jnp.einsum(
        "...cd,dh->...ch", received, w_gate[0], preferred_element_type=jnp.float32
    )
    up_act = jnp.einsum("...cd,dh->...ch", received, w_up[0], preferred_element_type=jnp.float32)
    hidden = (jax.nn.silu(gate_act) * up_act).astype(jnp.bfloat16)
    partial_out = jnp.einsum(
        "...ch,hd->...cd", hidden, w_down[0], preferred_element_type=jnp.float32
    ).astype(jnp.bfloat16)
    chip_sum = partial_out[0].astype(jnp.float32) + swap(partial_out[1], "c").astype(jnp.float32)
    expert_out = chip_sum[0] + swap(chip_sum[1].astype(jnp.bfloat16), "zl").astype(jnp.float32)
    returned = lax.all_to_all(
        expert_out.astype(jnp.bfloat16), CROSS, split_axis=0, concat_axis=0, tiled=True
    ).astype(jnp.float32)
    results = []
    for step in range(step_count):
        combined = jnp.dot(
            mix_table[step].reshape(row_count, -1),
            returned[:, step].reshape(-1, width),
            precision=lax.Precision.HIGHEST,
            preferred_element_type=jnp.float32,
        )
        results.append(combined.astype(jnp.bfloat16))
    return jnp.stack(results, 0)


def solution(mesh):
    devices = np.asarray(mesh.devices)
    dp, expert = devices.shape
    chip_mesh = Mesh(
        devices.reshape(dp, 4, expert // 16, 2, 2), ("dp", "x", "zh", "zl", "c")
    )
    rows_spec = P(None, ("dp", "x", "zh", "zl", "c"), None)
    blocks_spec = P(("dp", "x", "zh", "zl", "c"), None, None)
    placed = (rows_spec, rows_spec, rows_spec, blocks_spec, blocks_spec, blocks_spec)
    return jax.shard_map(
        body, mesh=chip_mesh, in_specs=placed, out_specs=rows_spec, check_vma=False
    )
```

```python
import jax
import jax.numpy as jnp
import numpy as np
from jax import lax
from jax.sharding import Mesh
from jax.sharding import PartitionSpec as P

EH = 1024
HS = 256
CROSS = ("x", "zh")


def route_tables(expert_ids, gate_codes, experts_all, capacity):
    step_count, row_count, top_count = expert_ids.shape
    flat = expert_ids.reshape(step_count, -1)
    order = jnp.arange(row_count * top_count, dtype=jnp.int32)
    earlier = order[None, :] < order[:, None]
    same = flat[:, :, None] == flat[:, None, :]
    slot_rank = jnp.sum(same & earlier, -1).reshape(expert_ids.shape)
    hit = (expert_ids[..., None, None] == jnp.arange(experts_all, dtype=jnp.int32)[:, None]) & (
        slot_rank[..., None, None] == jnp.arange(capacity, dtype=jnp.int32)
    )
    codes = gate_codes.astype(jnp.float32)
    gate_weight = codes / jnp.sum(codes, -1, keepdims=True)
    placement = jnp.sum(hit.astype(jnp.int32), 2)
    mix_table = jnp.sum(jnp.where(hit, gate_weight[..., None, None], 0.0), 2)
    return (placement, mix_table)


def swap(value, axis):
    return lax.ppermute(value, axis, [(0, 1), (1, 0)])


def body(tokens, expert_ids, gate_codes, w_gate, w_up, w_down):
    step_count, row_count, width = tokens.shape
    top_count = expert_ids.shape[2]
    experts_all = lax.axis_size(CROSS)
    capacity = min(row_count, max(2, 2 * row_count * top_count // experts_all))
    placement, mix_table = route_tables(expert_ids, gate_codes, experts_all, capacity)
    slots = jnp.einsum(
        "srec,srd->escd",
        placement.astype(jnp.bfloat16),
        tokens,
        preferred_element_type=jnp.float32,
    ).astype(jnp.bfloat16)
    received = lax.all_to_all(slots, CROSS, split_axis=0, concat_axis=0, tiled=True)
    received = jnp.stack([received, swap(received, "zl")], 0)
    received = jnp.stack([received, swap(received, "c")], 0)
    gate_act = jnp.einsum(
        "...cd,dh->...ch", received, w_gate[0], preferred_element_type=jnp.float32
    )
    up_act = jnp.einsum("...cd,dh->...ch", received, w_up[0], preferred_element_type=jnp.float32)
    hidden = (jax.nn.silu(gate_act) * up_act).astype(jnp.bfloat16)
    partial_out = jnp.einsum(
        "...ch,hd->...cd", hidden, w_down[0], preferred_element_type=jnp.float32
    ).astype(jnp.bfloat16)
    chip_sum = partial_out[0].astype(jnp.float32) + swap(partial_out[1], "c").astype(jnp.float32)
    expert_out = chip_sum[0] + swap(chip_sum[1].astype(jnp.bfloat16), "zl").astype(jnp.float32)
    returned = lax.all_to_all(
        expert_out.astype(jnp.bfloat16), CROSS, split_axis=0, concat_axis=0, tiled=True
    ).astype(jnp.float32)
    mixed = jnp.einsum(
        "srec,escd->srd",
        mix_table,
        returned,
        precision=lax.Precision.HIGHEST,
        preferred_element_type=jnp.float32,
    )
    return mixed.astype(jnp.bfloat16)


def solution(mesh):
    devices = np.asarray(mesh.devices)
    dp, expert = devices.shape
    chip_mesh = Mesh(
        devices.reshape(dp, 4, expert // 16, 2, 2), ("dp", "x", "zh", "zl", "c")
    )
    rows_spec = P(None, ("dp", "x", "zh", "zl", "c"), None)
    blocks_spec = P(("dp", "x", "zh", "zl", "c"), None, None)
    placed = (rows_spec, rows_spec, rows_spec, blocks_spec, blocks_spec, blocks_spec)
    return jax.shard_map(
        body, mesh=chip_mesh, in_specs=placed, out_specs=rows_spec, check_vma=False
    )
```

```python
import jax
import jax.numpy as jnp
import numpy as np
from jax import lax
from jax.sharding import Mesh
from jax.sharding import PartitionSpec as P

EH = 1024
HS = 256
CROSS = ("x", "zh")


def route_tables(expert_ids, gate_codes, experts_all, capacity):
    step_count, row_count, top_count = expert_ids.shape
    flat = expert_ids.reshape(step_count, -1)
    order = jnp.arange(row_count * top_count, dtype=jnp.int32)
    earlier = order[None, :] < order[:, None]
    same = flat[:, :, None] == flat[:, None, :]
    slot_rank = jnp.sum(same & earlier, -1).reshape(expert_ids.shape)
    hit = (expert_ids[..., None, None] == jnp.arange(experts_all, dtype=jnp.int32)[:, None]) & (
        slot_rank[..., None, None] == jnp.arange(capacity, dtype=jnp.int32)
    )
    codes = gate_codes.astype(jnp.float32)
    gate_weight = codes / jnp.sum(codes, -1, keepdims=True)
    placement = jnp.sum(hit.astype(jnp.int32), 2)
    mix_table = jnp.sum(jnp.where(hit, gate_weight[..., None, None], 0.0), 2)
    return (placement, mix_table)


def swap(value, axis):
    return lax.ppermute(value, axis, [(0, 1), (1, 0)])


def body(tokens, expert_ids, gate_codes, w_gate, w_up, w_down):
    step_count, row_count, width = tokens.shape
    top_count = expert_ids.shape[2]
    experts_all = lax.axis_size(CROSS)
    capacity = min(row_count, max(2, 2 * row_count * top_count // experts_all))
    placement, mix_table = route_tables(expert_ids, gate_codes, experts_all, capacity)
    slots = jnp.einsum(
        "srec,srd->escd",
        placement.astype(jnp.bfloat16),
        tokens,
        preferred_element_type=jnp.float32,
    ).astype(jnp.bfloat16)
    received = lax.all_to_all(slots, CROSS, split_axis=0, concat_axis=0, tiled=True)
    from_chip = swap(received, "zl")
    received = jnp.stack(
        [jnp.stack([received, from_chip], 0), jnp.stack([swap(received, "c"), swap(from_chip, "c")], 0)],
        0,
    )
    gate_act = jnp.einsum(
        "...cd,dh->...ch", received, w_gate[0], preferred_element_type=jnp.float32
    )
    up_act = jnp.einsum("...cd,dh->...ch", received, w_up[0], preferred_element_type=jnp.float32)
    hidden = (jax.nn.silu(gate_act) * up_act).astype(jnp.bfloat16)
    partial_out = jnp.einsum(
        "...ch,hd->...cd", hidden, w_down[0], preferred_element_type=jnp.float32
    ).astype(jnp.bfloat16)
    leaving = partial_out[0, 1].astype(jnp.float32) + swap(partial_out[1, 1], "c").astype(jnp.float32)
    arriving = swap(leaving.astype(jnp.bfloat16), "zl").astype(jnp.float32)
    staying = partial_out[0, 0].astype(jnp.float32) + swap(partial_out[1, 0], "c").astype(jnp.float32)
    expert_out = staying + arriving
    returned = lax.all_to_all(
        expert_out.astype(jnp.bfloat16), CROSS, split_axis=0, concat_axis=0, tiled=True
    ).astype(jnp.float32)
    mixed = jnp.einsum(
        "srec,escd->srd",
        mix_table,
        returned,
        precision=lax.Precision.HIGHEST,
        preferred_element_type=jnp.float32,
    )
    return mixed.astype(jnp.bfloat16)


def solution(mesh):
    devices = np.asarray(mesh.devices)
    dp, expert = devices.shape
    chip_mesh = Mesh(
        devices.reshape(dp, 4, expert // 16, 2, 2), ("dp", "x", "zh", "zl", "c")
    )
    rows_spec = P(None, ("dp", "x", "zh", "zl", "c"), None)
    blocks_spec = P(("dp", "x", "zh", "zl", "c"), None, None)
    placed = (rows_spec, rows_spec, rows_spec, blocks_spec, blocks_spec, blocks_spec)
    return jax.shard_map(
        body, mesh=chip_mesh, in_specs=placed, out_specs=rows_spec, check_vma=False
    )
```

```python
import jax
import jax.numpy as jnp
import numpy as np
from jax import lax
from jax.sharding import Mesh
from jax.sharding import PartitionSpec as P


CROSS = ("x", "zh")


def route_tables(expert_ids, gate_codes, experts_all, capacity):
    step_count, row_count, top_count = expert_ids.shape
    flat = expert_ids.reshape(step_count, -1)
    order = jnp.arange(row_count * top_count, dtype=jnp.int32)
    earlier = order[None, :] < order[:, None]
    same = flat[:, :, None] == flat[:, None, :]
    slot_rank = jnp.sum(same & earlier, -1).reshape(expert_ids.shape)
    hit = (expert_ids[..., None, None] == jnp.arange(experts_all, dtype=jnp.int32)[:, None]) & (
        slot_rank[..., None, None] == jnp.arange(capacity, dtype=jnp.int32)
    )
    codes = gate_codes.astype(jnp.float32)
    gate_weight = codes / jnp.sum(codes, -1, keepdims=True)
    placement = jnp.sum(hit.astype(jnp.int32), 2)
    mix_table = jnp.sum(jnp.where(hit, gate_weight[..., None, None], 0.0), 2)
    return (placement, mix_table)


def expert_mlp(rows, gate, up, down):
    gate_act = jnp.einsum("...d,dh->...h", rows, gate, preferred_element_type=jnp.float32)
    up_act = jnp.einsum("...d,dh->...h", rows, up, preferred_element_type=jnp.float32)
    hidden = (jax.nn.silu(gate_act) * up_act).astype(jnp.bfloat16)
    return jnp.einsum("...h,hd->...d", hidden, down, preferred_element_type=jnp.float32).astype(
        jnp.bfloat16
    )


def swap(value, axis):
    return lax.ppermute(value, axis, [(0, 1), (1, 0)])


def layer(tokens, expert_ids, gate_codes, w_gate, w_up, w_down):
    _, row_count, _ = tokens.shape
    top_count = expert_ids.shape[2]
    experts_all = lax.axis_size(CROSS)
    capacity = min(row_count, max(2, 2 * row_count * top_count // experts_all))
    placement, mix_table = route_tables(expert_ids, gate_codes, experts_all, capacity)
    slots = jnp.einsum(
        "srec,srd->escd",
        placement.astype(jnp.bfloat16),
        tokens,
        preferred_element_type=jnp.float32,
    ).astype(jnp.bfloat16)
    received = lax.all_to_all(slots, CROSS, split_axis=0, concat_axis=0, tiled=True)
    from_chip = swap(received, "zl")
    here = expert_mlp(jnp.stack([received, swap(received, "c")], 0), w_gate[0], w_up[0], w_down[0])
    staying = here[0].astype(jnp.float32) + swap(here[1], "c").astype(jnp.float32)
    there = expert_mlp(jnp.stack([from_chip, swap(from_chip, "c")], 0), w_gate[0], w_up[0], w_down[0])
    leaving = there[0].astype(jnp.float32) + swap(there[1], "c").astype(jnp.float32)
    arriving = swap(leaving.astype(jnp.bfloat16), "zl").astype(jnp.float32)
    expert_out = staying + arriving
    returned = lax.all_to_all(
        expert_out.astype(jnp.bfloat16), CROSS, split_axis=0, concat_axis=0, tiled=True
    ).astype(jnp.float32)
    mixed = jnp.einsum(
        "srec,escd->srd",
        mix_table,
        returned,
        precision=lax.Precision.HIGHEST,
        preferred_element_type=jnp.float32,
    )
    return mixed.astype(jnp.bfloat16)


def solution(mesh):
    devices = np.asarray(mesh.devices)
    dp, expert = devices.shape
    chip_mesh = Mesh(
        devices.reshape(dp, 4, expert // 16, 2, 2), ("dp", "x", "zh", "zl", "c")
    )
    rows_spec = P(None, ("dp", "x", "zh", "zl", "c"), None)
    blocks_spec = P(("dp", "x", "zh", "zl", "c"), None, None)
    placed = (rows_spec, rows_spec, rows_spec, blocks_spec, blocks_spec, blocks_spec)
    return jax.shard_map(
        layer, mesh=chip_mesh, in_specs=placed, out_specs=rows_spec, check_vma=False
    )
```

```python
import jax
import jax.numpy as jnp
import numpy as np
from jax import lax
from jax.sharding import Mesh
from jax.sharding import PartitionSpec as P


CROSS = ("x", "zh")


def route_tables(expert_ids, gate_codes, experts_all, capacity):
    step_count, row_count, top_count = expert_ids.shape
    flat = expert_ids.reshape(step_count, -1)
    order = jnp.arange(row_count * top_count, dtype=jnp.int32)
    earlier = order[None, :] < order[:, None]
    same = flat[:, :, None] == flat[:, None, :]
    slot_rank = jnp.sum(same & earlier, -1).reshape(expert_ids.shape)
    hit = (expert_ids[..., None, None] == jnp.arange(experts_all, dtype=jnp.int32)[:, None]) & (
        slot_rank[..., None, None] == jnp.arange(capacity, dtype=jnp.int32)
    )
    codes = gate_codes.astype(jnp.float32)
    gate_weight = codes / jnp.sum(codes, -1, keepdims=True)
    placement = jnp.sum(hit.astype(jnp.int32), 2)
    mix_table = jnp.sum(jnp.where(hit, gate_weight[..., None, None], 0.0), 2)
    return (placement, mix_table)


def mix_of(expert_ids, gate_codes, experts_all, capacity):
    return route_tables(lax.optimization_barrier(expert_ids), gate_codes, experts_all, capacity)[1]


def expert_mlp(rows, gate, up, down):
    gate_act = jnp.einsum("...d,dh->...h", rows, gate, preferred_element_type=jnp.float32)
    up_act = jnp.einsum("...d,dh->...h", rows, up, preferred_element_type=jnp.float32)
    hidden = (jax.nn.silu(gate_act) * up_act).astype(jnp.bfloat16)
    return jnp.einsum("...h,hd->...d", hidden, down, preferred_element_type=jnp.float32).astype(
        jnp.bfloat16
    )


def swap(value, axis):
    return lax.ppermute(value, axis, [(0, 1), (1, 0)])


def layer(tokens, expert_ids, gate_codes, w_gate, w_up, w_down):
    _, row_count, _ = tokens.shape
    top_count = expert_ids.shape[2]
    experts_all = lax.axis_size(CROSS)
    capacity = min(row_count, max(2, 2 * row_count * top_count // experts_all))
    placement = route_tables(expert_ids, gate_codes, experts_all, capacity)[0]
    slots = jnp.einsum(
        "srec,srd->escd",
        placement.astype(jnp.bfloat16),
        tokens,
        preferred_element_type=jnp.float32,
    ).astype(jnp.bfloat16)
    received = lax.all_to_all(slots, CROSS, split_axis=0, concat_axis=0, tiled=True)
    from_chip = swap(received, "zl")
    mix_table = mix_of(expert_ids, gate_codes, experts_all, capacity)
    here = expert_mlp(jnp.stack([received, swap(received, "c")], 0), w_gate[0], w_up[0], w_down[0])
    staying = here[0].astype(jnp.float32) + swap(here[1], "c").astype(jnp.float32)
    there = expert_mlp(jnp.stack([from_chip, swap(from_chip, "c")], 0), w_gate[0], w_up[0], w_down[0])
    leaving = there[0].astype(jnp.float32) + swap(there[1], "c").astype(jnp.float32)
    arriving = swap(leaving.astype(jnp.bfloat16), "zl").astype(jnp.float32)
    expert_out = staying + arriving
    returned = lax.all_to_all(
        expert_out.astype(jnp.bfloat16), CROSS, split_axis=0, concat_axis=0, tiled=True
    ).astype(jnp.float32)
    mixed = jnp.einsum(
        "srec,escd->srd",
        mix_table,
        returned,
        precision=lax.Precision.HIGHEST,
        preferred_element_type=jnp.float32,
    )
    return mixed.astype(jnp.bfloat16)


def solution(mesh):
    devices = np.asarray(mesh.devices)
    dp, expert = devices.shape
    chip_mesh = Mesh(
        devices.reshape(dp, 4, expert // 16, 2, 2), ("dp", "x", "zh", "zl", "c")
    )
    rows_spec = P(None, ("dp", "x", "zh", "zl", "c"), None)
    blocks_spec = P(("dp", "x", "zh", "zl", "c"), None, None)
    placed = (rows_spec, rows_spec, rows_spec, blocks_spec, blocks_spec, blocks_spec)
    return jax.shard_map(
        layer, mesh=chip_mesh, in_specs=placed, out_specs=rows_spec, check_vma=False
    )
```

```python
import jax
import jax.numpy as jnp
import numpy as np
from jax import lax
from jax.sharding import Mesh
from jax.sharding import PartitionSpec as P


CROSS = ("x", "zh")


def route_tables(expert_ids, gate_codes, experts_all, capacity):
    step_count, row_count, top_count = expert_ids.shape
    flat = expert_ids.reshape(step_count, -1)
    order = jnp.arange(row_count * top_count, dtype=jnp.int32)
    earlier = order[None, :] < order[:, None]
    same = flat[:, :, None] == flat[:, None, :]
    slot_rank = jnp.sum(same & earlier, -1).reshape(expert_ids.shape)
    hit = (expert_ids[..., None, None] == jnp.arange(experts_all, dtype=jnp.int32)[:, None]) & (
        slot_rank[..., None, None] == jnp.arange(capacity, dtype=jnp.int32)
    )
    codes = gate_codes.astype(jnp.float32)
    gate_weight = codes / jnp.sum(codes, -1, keepdims=True)
    placement = jnp.sum(hit.astype(jnp.int32), 2)
    mix_table = jnp.sum(jnp.where(hit, gate_weight[..., None, None], 0.0), 2)
    return (placement, mix_table)


def mix_of(expert_ids, gate_codes, experts_all, capacity):
    return route_tables(lax.optimization_barrier(expert_ids), gate_codes, experts_all, capacity)[1]


def expert_mlp(rows, gate, up, down):
    gate_act = jnp.einsum("...d,dh->...h", rows, gate, preferred_element_type=jnp.float32)
    up_act = jnp.einsum("...d,dh->...h", rows, up, preferred_element_type=jnp.float32)
    hidden = (jax.nn.silu(gate_act) * up_act).astype(jnp.bfloat16)
    return jnp.einsum("...h,hd->...d", hidden, down, preferred_element_type=jnp.float32).astype(
        jnp.bfloat16
    )


def swap(value, axis):
    return lax.ppermute(value, axis, [(0, 1), (1, 0)])


def layer(tokens, expert_ids, gate_codes, w_gate, w_up, w_down):
    _, row_count, _ = tokens.shape
    top_count = expert_ids.shape[2]
    experts_all = lax.axis_size(CROSS)
    capacity = min(row_count, max(2, 2 * row_count * top_count // experts_all))
    placement = route_tables(expert_ids, gate_codes, experts_all, capacity)[0]
    slots = jnp.einsum(
        "srec,srd->escd",
        placement.astype(jnp.bfloat16),
        tokens,
        preferred_element_type=jnp.float32,
    ).astype(jnp.bfloat16)
    received = lax.all_to_all(slots, CROSS, split_axis=0, concat_axis=0, tiled=True)
    from_chip = swap(received, "zl")
    mix_table = mix_of(expert_ids, gate_codes, experts_all, capacity)
    here = expert_mlp(jnp.stack([received, swap(received, "c")], 0), w_gate[0], w_up[0], w_down[0])
    staying = here[0].astype(jnp.float32) + swap(here[1], "c").astype(jnp.float32)
    from_chip_other = swap(from_chip, "c")
    there_own = expert_mlp(from_chip, w_gate[0], w_up[0], w_down[0])
    there_other = expert_mlp(from_chip_other, w_gate[0], w_up[0], w_down[0])
    leaving = there_own.astype(jnp.float32) + swap(there_other, "c").astype(jnp.float32)
    arriving = swap(leaving.astype(jnp.bfloat16), "zl").astype(jnp.float32)
    expert_out = staying + arriving
    returned = lax.all_to_all(
        expert_out.astype(jnp.bfloat16), CROSS, split_axis=0, concat_axis=0, tiled=True
    ).astype(jnp.float32)
    mixed = jnp.einsum(
        "srec,escd->srd",
        mix_table,
        returned,
        precision=lax.Precision.HIGHEST,
        preferred_element_type=jnp.float32,
    )
    return mixed.astype(jnp.bfloat16)


def solution(mesh):
    devices = np.asarray(mesh.devices)
    dp, expert = devices.shape
    chip_mesh = Mesh(
        devices.reshape(dp, 4, expert // 16, 2, 2), ("dp", "x", "zh", "zl", "c")
    )
    rows_spec = P(None, ("dp", "x", "zh", "zl", "c"), None)
    blocks_spec = P(("dp", "x", "zh", "zl", "c"), None, None)
    placed = (rows_spec, rows_spec, rows_spec, blocks_spec, blocks_spec, blocks_spec)
    return jax.shard_map(
        layer, mesh=chip_mesh, in_specs=placed, out_specs=rows_spec, check_vma=False
    )
```
